32 devices in a mesh: groups: 2 (over y), graph: 16 (over z, x, core).
Axes of the slice: x: 2, y: 2, z: 4, core: 2. Of those that a mesh axis runs over, the one named last changes fastest.
Arguments:
- tile_weight: bfloat16 [64, 8, 128, 128], P('graph'), may hold values from 0.00018310547 to 0.0018310547
- tile_cols: int32 [64, 8], P('graph'), may hold values from 0 to 63, as said below
- far_weight: bfloat16 [8192, 64], P('graph'), may hold values from 0.00018310547 to 0.0018310547
- send_rows: int32 [256, 4], P('graph'), may hold values from 0 to 511, as said below
- dest_links: int32 [1024], P('groups'), parts along dimension 0, may hold values from 0 to 8191
- demand: int32 [16384, 512], P(('groups', 'graph')), parts along dimension 0, may hold values from 0 to 3
- values_start: float32 [16384, 512], P(('groups', 'graph')), parts along dimension 0, may hold values from 0.15 to 6.6
Outputs:
- values: float32 [16384, 512], P(('groups', 'graph')), parts along dimension 0
- flows: float32 [16384], P(('groups', 'graph')), parts along dimension 0
The draws below stay inside these ranges and needn't reach their ends.
There are 2 independent parts, one for each index of `groups`. The reference program is written for one: setup_inputs(seed, part) draws one part's arguments, and reference() takes and returns one part's arrays. A program takes and returns all parts, laid end to end along the dimension named above; an argument that names none is the same for every part. Nothing has to cross between parts.
Inputs may be any that keep to these rules, and one draw needn't show every extreme that they name: `tile_cols`: row tile t of device p = t // 4 has column tiles among p*4 - 1 to (p+1)*4, clipped to the range of tiles; each device's first row tile reads the tile just before its own, and its last row tile the tile just after. `send_rows`: local link numbers on the sending device.
All inputs are finite; a program needn't handle non-finite values.
Results may differ from the reference program's by a relative error of at most 0.0003.
Values may be sent and summed in bfloat16 or wider, within the bound.
No kernel may reach another device: no remote copies, remote signals or barrier semaphores. Data moves between devices by JAX's collectives and lax.ppermute only.
A program may use at most 128 MiB of HBM per device.

```python
import math
import jax
import jax.numpy as jnp
from jax import lax

TILE = 128
DEST = 512
TILES_DEV = 4
NBRS = 8
SEND = 4
SWEEPS = 3
LINK_DEV = 512
TILES = 64
LINKS = 8192
FAR = 64
N_GRAPH = 16


def draw_tile_cols(key, part):
    base = jnp.arange(TILES, dtype=jnp.int32) // TILES_DEV * TILES_DEV
    offset = jax.random.randint(key, (TILES, NBRS), -1, TILES_DEV + 1)
    columns = base[:, None] + offset
    position = jnp.arange(TILES, dtype=jnp.int32) % TILES_DEV
    columns = columns.at[:, 0].set(jnp.where(position == 0, base - 1, columns[:, 0]))
    columns = columns.at[:, 1].set(jnp.where(position == TILES_DEV - 1, base + TILES_DEV, columns[:, 1]))
    return jnp.clip(columns, 0, TILES - 1).astype(jnp.int32)


def draw_send_rows(key, part):
    picked = jax.random.randint(key, (N_GRAPH * N_GRAPH, SEND), 0, LINK_DEV)
    picked = picked.at[0, 0].set(0)
    picked = picked.at[N_GRAPH * N_GRAPH - 1, SEND - 1].set(LINK_DEV - 1)
    return picked.astype(jnp.int32)


def draw_values_start(key, part):
    center_key = jax.random.fold_in(key, 11)
    width_key = jax.random.fold_in(key, 12)
    rough_key = jax.random.fold_in(key, 13)
    center = jax.random.randint(center_key, (DEST,), 0, LINKS)
    width = jnp.exp(jax.random.uniform(width_key, (DEST,), jnp.float32, math.log(1.0 * LINK_DEV), math.log(0.5 * LINKS)))
    link_ids = jnp.arange(LINKS, dtype=jnp.int32)
    gap = jnp.abs(link_ids[:, None] - center[None, :])
    gap = jnp.minimum(gap, LINKS - gap).astype(jnp.float32)
    bump = 0.3 + 3.0 * jnp.exp(-4.6 * gap / width[None, :])
    rough = jnp.exp(jax.random.uniform(rough_key, (LINKS, DEST), jnp.float32, math.log(0.5), math.log(2.0)))
    return (rough * bump).astype(jnp.float32)


def with_ends(drawn, own_key, smallest, high):
    longest = drawn.shape.index(max(drawn.shape))
    spots = []
    for shift in (0, 1):
        where = [jax.random.randint(jax.random.fold_in(own_key, axis), (), 0, length) for axis, length in enumerate(drawn.shape)]
        where[longest] = (where[longest] + shift) % drawn.shape[longest]
        spots.append(tuple(where))
    return drawn.at[spots[0]].set(smallest).at[spots[1]].set(high)


def shard_levels(key, extent, shards, least, top_value):
    gain = 1.0
    for axis_at, shards_of in shards:
        steps = jax.random.uniform(jax.random.fold_in(jax.random.fold_in(key, 6), axis_at), (shards_of,), jnp.float32, least / len(shards), top_value / len(shards))
        gain = gain * jnp.repeat(jnp.exp(steps), extent[axis_at] // shards_of).reshape((-1,) + (1,) * (len(extent) - 1 - axis_at))
    return gain


def setup_inputs(seed: int = 0, part: int = 0) -> dict:
    keys = jax.random.split(jax.random.key(seed), 8)
    own_keys = jax.random.split(jax.random.fold_in(keys[7], part), 8)
    return {
        "tile_weight": jnp.clip(jnp.exp(math.log(0.0018310547) - 2.3025851 * jax.random.uniform(keys[0], (TILES, NBRS, TILE, TILE), jnp.float32) ** shard_levels(keys[0], (TILES, NBRS, TILE, TILE), ((0, 16),), -0.2, 0.2)), 0.00018310547, 0.0018310547).astype(jnp.bfloat16),
        "tile_cols": draw_tile_cols(jax.random.fold_in(keys[7], 71), part),
        "far_weight": jnp.clip(jnp.exp(math.log(0.0018310547) - 2.3025851 * jax.random.uniform(keys[2], (LINKS, FAR), jnp.float32) ** shard_levels(keys[2], (LINKS, FAR), ((0, 16),), -0.2, 0.2)), 0.00018310547, 0.0018310547).astype(jnp.bfloat16),
        "send_rows": draw_send_rows(jax.random.fold_in(keys[7], 71), part),
        "dest_links": with_ends(jax.random.randint(own_keys[4], (DEST,), 0, LINKS), jax.random.fold_in(own_keys[4], 1), 0, LINKS - 1).astype(jnp.int32),
        "demand": with_ends(jax.random.randint(own_keys[5], (LINKS, DEST), 0, 4), jax.random.fold_in(own_keys[5], 1), 0, 3).astype(jnp.int32),
        "values_start": draw_values_start(jax.random.fold_in(jax.random.fold_in(keys[7], part), 71), part),
    }


def reference(tile_weight, tile_cols, far_weight, send_rows, dest_links, demand, values_start):
    peer_count = N_GRAPH
    links_here = TILES_DEV * TILE
    link_ids = jnp.arange(LINKS, dtype=jnp.int32)
    dest_mask = (link_ids[:, None] == dest_links[None, :]).astype(jnp.float32)
    demand_flow = demand.astype(jnp.float32)
    source = jnp.arange(peer_count, dtype=jnp.int32)[:, None, None] * links_here + send_rows.reshape(peer_count, peer_count, SEND)
    far_index = jnp.transpose(source, (1, 0, 2)).reshape(peer_count, peer_count * SEND).astype(jnp.int32)
    weight_dev = tile_weight.reshape(peer_count, TILES_DEV, NBRS, TILE, TILE)
    cols_dev = tile_cols.reshape(peer_count, TILES_DEV, NBRS)
    far_dev = far_weight.reshape(peer_count, links_here, FAR)

    def value_sweep(values):
        narrow = values.astype(jnp.bfloat16)
        narrow_tiles = narrow.reshape(TILES, TILE, DEST)

        def one_device(pieces):
            weight_part, cols_part, far_part, index_part = pieces
            picked = narrow_tiles[cols_part].astype(jnp.float32)
            near = jnp.einsum("tkij,tkjd->tid", weight_part.astype(jnp.float32), picked).reshape(links_here, DEST)
            far = jnp.dot(far_part, narrow[index_part], preferred_element_type=jnp.float32)
            return near + far

        total = lax.map(one_device, (weight_dev, cols_dev, far_dev, far_index))
        return total.reshape(LINKS, DEST) + dest_mask

    values = values_start.astype(jnp.float32)
    for sweep_idx in range(SWEEPS):
        values = value_sweep(values)

    def load_sweep(load_now):
        ratio = (load_now / values).astype(jnp.bfloat16)
        ratio_dev = ratio.reshape(peer_count, TILES_DEV, TILE, DEST)

        def add_device(accum, pieces):
            weight_part, cols_part, far_part, index_part, ratio_part = pieces
            spread = jnp.einsum("tkij,tid->tkjd", weight_part.astype(jnp.float32), ratio_part.astype(jnp.float32))
            tiled = accum.reshape(TILES, TILE, DEST).at[cols_part.reshape(-1)].add(spread.reshape(-1, TILE, DEST))
            far = jnp.dot(far_part.T, ratio_part.reshape(links_here, DEST), preferred_element_type=jnp.float32)
            return tiled.reshape(LINKS, DEST).at[index_part].add(far), None

        start = jnp.zeros((LINKS, DEST), jnp.float32)
        total, unused = lax.scan(add_device, start, (weight_dev, cols_dev, far_dev, far_index, ratio_dev))
        return values * total + demand_flow

    load = demand_flow
    for sweep_idx in range(SWEEPS):
        load = load_sweep(load)
    flows = jnp.mean(load, axis=1)
    return values, flows
```

```python
import jax
import jax.numpy as jnp
from jax import lax
from jax.sharding import PartitionSpec as P

SWEEPS = 3


def passed_along(value, axis, steps):
    count = lax.axis_size(axis)
    leading, last = (max(0, -steps), min(count, count - steps))
    return lax.ppermute(value, axis, [(source, source + steps) for source in range(leading, last)])


def split_high_low(dense):
    high = lax.optimization_barrier(dense.astype(jnp.bfloat16))
    low = (dense - high.astype(jnp.float32)).astype(jnp.bfloat16)
    return high, low


def shards(tile_weight, tile_cols, far_weight, send_rows, dest_links, demand, values_start):
    tiles_here, nbrs, tile_size, _ = tile_weight.shape
    links_here = tiles_here * tile_size
    dest_count = demand.shape[1]
    peer_count = lax.axis_size("graph")
    slot_count = send_rows.shape[1]
    span = tiles_here + 2
    own_index = lax.axis_index("graph")
    local_cols = tile_cols - own_index * tiles_here + 1
    link_ids = own_index * links_here + jnp.arange(links_here, dtype=jnp.int32)
    dest_mask = (link_ids[:, None] == dest_links[None, :]).astype(jnp.float32)
    demand_flow = demand.astype(jnp.float32)
    tile_pick = (
        local_cols[:, :, None] == jnp.arange(span, dtype=jnp.int32)[None, None, :]
    ).astype(jnp.bfloat16)
    dense = jnp.einsum("tks,tkij->tisj", tile_pick, tile_weight, preferred_element_type=jnp.float32)
    dense = dense.reshape(links_here, span * tile_size)
    w_high, w_low = split_high_low(dense)
    wt_high = w_high.T
    wt_low = w_low.T
    send_flat = send_rows.reshape(-1)
    row_pick = (jnp.arange(links_here, dtype=jnp.int32)[:, None] == send_flat[None, :]).astype(
        jnp.bfloat16
    )
    row_pick_t = row_pick.T

    values = values_start
    for sweep_idx in range(SWEEPS):
        narrow = values.astype(jnp.bfloat16)
        head = narrow[:tile_size]
        tail = narrow[links_here - tile_size :]
        outgoing = jnp.dot(row_pick_t, narrow, preferred_element_type=jnp.float32).astype(jnp.bfloat16)
        outgoing = outgoing.reshape(peer_count, slot_count, dest_count)
        received = lax.all_to_all(outgoing, "graph", split_axis=0, concat_axis=0, tiled=True)
        from_prev = passed_along(tail, "graph", 1)
        from_next = passed_along(head, "graph", -1)
        padded = jnp.concatenate([from_prev, narrow, from_next], axis=0)
        near = jnp.dot(w_high, padded, preferred_element_type=jnp.float32) + jnp.dot(
            w_low, padded, preferred_element_type=jnp.float32
        )
        flat = received.reshape(-1, dest_count)
        far = jnp.dot(far_weight, flat, preferred_element_type=jnp.float32)
        values = near + far + dest_mask

    load = demand_flow
    rest_rows = links_here - tile_size
    for sweep_idx in range(SWEEPS):
        ratio = (load / values).astype(jnp.bfloat16)
        landed = jnp.dot(wt_high, ratio, preferred_element_type=jnp.float32) + jnp.dot(
            wt_low, ratio, preferred_element_type=jnp.float32
        )
        lower_rim = landed[:tile_size].astype(jnp.bfloat16)
        upper_rim = landed[tile_size + links_here :].astype(jnp.bfloat16)
        own_part = landed[tile_size : tile_size + links_here]
        far_part = lax.dot_general(
            far_weight, ratio, (((0,), (0,)), ((), ())), preferred_element_type=jnp.float32
        )
        far_part = far_part.astype(jnp.bfloat16).reshape(peer_count, slot_count, dest_count)
        returned = lax.all_to_all(far_part, "graph", split_axis=0, concat_axis=0, tiled=True)
        from_next = passed_along(lower_rim, "graph", -1).astype(jnp.float32)
        from_prev = passed_along(upper_rim, "graph", 1).astype(jnp.float32)
        own_part = (
            own_part
            + jnp.pad(from_prev, ((0, rest_rows), (0, 0)))
            + jnp.pad(from_next, ((rest_rows, 0), (0, 0)))
        )
        far_in = jnp.dot(row_pick, returned.reshape(-1, dest_count), preferred_element_type=jnp.float32)
        load = values * (own_part + far_in) + demand_flow
    flows = jnp.mean(load, axis=1)
    return (values, flows)


def solution(mesh):
    return jax.shard_map(
        shards,
        mesh=mesh,
        in_specs=(
            P("graph", None, None, None),
            P("graph", None),
            P("graph", None),
            P("graph", None),
            P("groups"),
            P(("groups", "graph"), None),
            P(("groups", "graph"), None),
        ),
        out_specs=(P(("groups", "graph"), None), P(("groups", "graph"))),
        check_vma=False,
    )
```

```python
import jax
import jax.numpy as jnp
from jax import lax
from jax.sharding import PartitionSpec as P

SWEEPS = 3


def passed_along(value, axis, steps):
    count = lax.axis_size(axis)
    return lax.ppermute(value, axis, [(source, (source + steps) % count) for source in range(count)])


def split_high_low(dense):
    high = lax.optimization_barrier(dense.astype(jnp.bfloat16))
    low = (dense - high.astype(jnp.float32)).astype(jnp.bfloat16)
    return high, low


def shards(tile_weight, tile_cols, far_weight, send_rows, dest_links, demand, values_start):
    tiles_here, nbrs, tile_size, _ = tile_weight.shape
    links_here = tiles_here * tile_size
    dest_count = demand.shape[1]
    peer_count = lax.axis_size("graph")
    slot_count = send_rows.shape[1]
    span = tiles_here + 2
    own_index = lax.axis_index("graph")
    local_cols = tile_cols - own_index * tiles_here + 1
    link_ids = own_index * links_here + jnp.arange(links_here, dtype=jnp.int32)
    dest_mask = (link_ids[:, None] == dest_links[None, :]).astype(jnp.float32)
    demand_flow = demand.astype(jnp.float32)
    tile_pick = (
        local_cols[:, :, None] == jnp.arange(span, dtype=jnp.int32)[None, None, :]
    ).astype(jnp.bfloat16)
    dense = jnp.einsum("tks,tkij->tisj", tile_pick, tile_weight, preferred_element_type=jnp.float32)
    dense = dense.reshape(links_here, span * tile_size)
    w_high, w_low = split_high_low(dense)
    wt_high = w_high.T
    wt_low = w_low.T
    send_flat = send_rows.reshape(-1)
    row_pick = (jnp.arange(links_here, dtype=jnp.int32)[:, None] == send_flat[None, :]).astype(
        jnp.bfloat16
    )
    row_pick_t = row_pick.T

    values = values_start
    for sweep_idx in range(SWEEPS):
        narrow = values.astype(jnp.bfloat16)
        head = narrow[:tile_size]
        tail = narrow[links_here - tile_size :]
        outgoing = jnp.dot(row_pick_t, narrow, preferred_element_type=jnp.float32).astype(jnp.bfloat16)
        outgoing = outgoing.reshape(peer_count, slot_count, dest_count)
        received = lax.all_to_all(outgoing, "graph", split_axis=0, concat_axis=0, tiled=True)
        from_prev = passed_along(tail, "graph", 1)
        from_next = passed_along(head, "graph", -1)
        padded = jnp.concatenate([from_prev, narrow, from_next], axis=0)
        near = jnp.dot(w_high, padded, preferred_element_type=jnp.float32) + jnp.dot(
            w_low, padded, preferred_element_type=jnp.float32
        )
        flat = received.reshape(-1, dest_count)
        far = jnp.dot(far_weight, flat, preferred_element_type=jnp.float32)
        values = near + far + dest_mask

    load = demand_flow
    rest_rows = links_here - tile_size
    for sweep_idx in range(SWEEPS):
        ratio = (load / values).astype(jnp.bfloat16)
        landed = jnp.dot(wt_high, ratio, preferred_element_type=jnp.float32) + jnp.dot(
            wt_low, ratio, preferred_element_type=jnp.float32
        )
        lower_rim = landed[:tile_size].astype(jnp.bfloat16)
        upper_rim = landed[tile_size + links_here :].astype(jnp.bfloat16)
        own_part = landed[tile_size : tile_size + links_here]
        far_part = lax.dot_general(
            far_weight, ratio, (((0,), (0,)), ((), ())), preferred_element_type=jnp.float32
        )
        far_part = far_part.astype(jnp.bfloat16).reshape(peer_count, slot_count, dest_count)
        returned = lax.all_to_all(far_part, "graph", split_axis=0, concat_axis=0, tiled=True)
        from_next = passed_along(lower_rim, "graph", -1).astype(jnp.float32)
        from_prev = passed_along(upper_rim, "graph", 1).astype(jnp.float32)
        own_part = (
            own_part
            + jnp.pad(from_prev, ((0, rest_rows), (0, 0)))
            + jnp.pad(from_next, ((rest_rows, 0), (0, 0)))
        )
        far_in = jnp.dot(row_pick, returned.reshape(-1, dest_count), preferred_element_type=jnp.float32)
        load = values * (own_part + far_in) + demand_flow
    flows = jnp.mean(load, axis=1)
    return (values, flows)


def solution(mesh):
    return jax.shard_map(
        shards,
        mesh=mesh,
        in_specs=(
            P("graph", None, None, None),
            P("graph", None),
            P("graph", None),
            P("graph", None),
            P("groups"),
            P(("groups", "graph"), None),
            P(("groups", "graph"), None),
        ),
        out_specs=(P(("groups", "graph"), None), P(("groups", "graph"))),
        check_vma=False,
    )
```

```python
import jax
import jax.numpy as jnp
from jax import lax
from jax.sharding import PartitionSpec as P

SWEEPS = 3


def passed_along(value, axis, steps):
    count = lax.axis_size(axis)
    return lax.ppermute(value, axis, [(source, (source + steps) % count) for source in range(count)])


def split_high_low(dense):
    high = lax.optimization_barrier(dense.astype(jnp.bfloat16))
    low = (dense - high.astype(jnp.float32)).astype(jnp.bfloat16)
    return high, low


def shards(tile_weight, tile_cols, far_weight, send_rows, dest_links, demand, values_start):
    tiles_here, nbrs, tile_size, _ = tile_weight.shape
    links_here = tiles_here * tile_size
    dest_count = demand.shape[1]
    peer_count = lax.axis_size("graph")
    slot_count = send_rows.shape[1]
    span = tiles_here + 2
    own_index = lax.axis_index("graph")
    local_cols = tile_cols - own_index * tiles_here + 1
    link_ids = own_index * links_here + jnp.arange(links_here, dtype=jnp.int32)
    dest_mask = (link_ids[:, None] == dest_links[None, :]).astype(jnp.float32)
    demand_flow = demand.astype(jnp.float32)
    tile_pick = (
        local_cols[:, :, None] == jnp.arange(span, dtype=jnp.int32)[None, None, :]
    ).astype(jnp.bfloat16)
    dense = jnp.einsum("tks,tkij->tisj", tile_pick, tile_weight, preferred_element_type=jnp.float32)
    dense = dense.reshape(links_here, span * tile_size)
    w_high, w_low = split_high_low(dense)
    send_flat = send_rows.reshape(-1)
    row_pick = (jnp.arange(links_here, dtype=jnp.int32)[:, None] == send_flat[None, :]).astype(
        jnp.bfloat16
    )
    peers = send_rows.shape[0]
    row_pick3 = row_pick.reshape(links_here, peers, slot_count)
    far_weight3 = far_weight.reshape(links_here, peers, slot_count)
    far_slots = far_weight.shape[1]
    w_value = jnp.concatenate([w_high, w_low], axis=1)
    w_load = jnp.concatenate([w_high.T, w_low.T], axis=1)

    values = values_start
    for sweep_idx in range(SWEEPS):
        narrow = values.astype(jnp.bfloat16)
        head = narrow[:tile_size]
        tail = narrow[links_here - tile_size :]
        outgoing = jnp.einsum(
            "lps,ld->psd", row_pick3, narrow, preferred_element_type=jnp.float32
        ).astype(jnp.bfloat16)
        received = lax.all_to_all(outgoing, "graph", split_axis=0, concat_axis=0, tiled=True)
        from_prev = passed_along(tail, "graph", 1)
        from_next = passed_along(head, "graph", -1)
        stacked = jnp.concatenate(
            [from_prev, narrow, from_next, from_prev, narrow, from_next], axis=0
        )
        far = jnp.einsum("lps,psd->ld", far_weight3, received, preferred_element_type=jnp.float32)
        values = jnp.dot(w_value, stacked, preferred_element_type=jnp.float32) + far + dest_mask

    load = demand_flow
    rest_rows = links_here - tile_size
    span_rows = span * tile_size
    for sweep_idx in range(SWEEPS):
        ratio = (load / values).astype(jnp.bfloat16)
        landed = jnp.dot(
            w_load, jnp.concatenate([ratio, ratio], axis=0), preferred_element_type=jnp.float32
        )
        lower_rim = landed[:tile_size].astype(jnp.bfloat16)
        upper_rim = landed[tile_size + links_here : span_rows].astype(jnp.bfloat16)
        own_part = landed[tile_size : tile_size + links_here]
        far_part = jnp.einsum(
            "lps,ld->psd", far_weight3, ratio, preferred_element_type=jnp.float32
        ).astype(jnp.bfloat16)
        returned = lax.all_to_all(far_part, "graph", split_axis=0, concat_axis=0, tiled=True)
        from_next = passed_along(lower_rim, "graph", -1).astype(jnp.float32)
        from_prev = passed_along(upper_rim, "graph", 1).astype(jnp.float32)
        own_part = (
            own_part
            + jnp.pad(from_prev, ((0, rest_rows), (0, 0)))
            + jnp.pad(from_next, ((rest_rows, 0), (0, 0)))
        )
        far_in = jnp.einsum("lps,psd->ld", row_pick3, returned, preferred_element_type=jnp.float32)
        load = values * (own_part + far_in) + demand_flow
    flows = jnp.mean(load, axis=1)
    return (values, flows)


def solution(mesh):
    return jax.shard_map(
        shards,
        mesh=mesh,
        in_specs=(
            P("graph", None, None, None),
            P("graph", None),
            P("graph", None),
            P("graph", None),
            P("groups"),
            P(("groups", "graph"), None),
            P(("groups", "graph"), None),
        ),
        out_specs=(P(("groups", "graph"), None), P(("groups", "graph"))),
        check_vma=False,
    )
```
